256 devices in a mesh: sec: 16 (over y, x), bulk: 16 (over z, core).
Axes of the slice: x: 4, y: 4, z: 8, core: 2. Of those that a mesh axis runs over, the one named last changes fastest.
Arguments:
- modes_x: bfloat16 [96, 16, 64, 8, 128], P(None, 'sec', 'bulk'), may hold values from -30 to 30
- modes_p: bfloat16 [96, 16, 64, 8, 128], P(None, 'sec', 'bulk'), may hold values from -30 to 30
- ritz_values: float32 [96], replicated, may hold values from 0.05 to 2
- node_types: int32 [16, 64, 8, 128], P('sec', 'bulk'), may hold values from 0 to 7
- stiff_table: float32 [8], replicated, may hold values from 1 to 10
- mass_table: float32 [8], replicated, may hold values from 0.5 to 4
- joint_nodes: int32 [16, 16, 16, 128], P('sec', 'bulk'), may hold values from 0 to 4095
- joint_count: int32 [16, 16, 16], P('sec', 'bulk'), may hold values from 0 to 128, as said below
Outputs:
- search_dir: bfloat16 [96, 16, 64, 8, 128], P(None, 'sec', 'bulk')
- ritz_pencil: float32 [288, 288], replicated
The draws below stay inside these ranges and needn't reach their ends.
Inputs may be any that keep to these rules, and one draw needn't show every extreme that they name: `joint_nodes`: local node numbers of a slab; slots at or beyond the count are ignored; a node may appear in several slots. Symmetric: joint_count[a, b, c] = joint_count[c, b, a], zero for a = c.
All inputs are finite; a program needn't handle non-finite values.
Results may differ from the reference program's by a relative error of at most 0.0004.
The reference program's roundings to bfloat16 on the way (of `kappa` and `span`) count: a program that leaves them out, or rounds other values in their place, can miss the bound.
Values may be sent and summed in bfloat16 or wider, within the bound.
No kernel may reach another device: no remote copies, remote signals or barrier semaphores. Data moves between devices by JAX's collectives and lax.ppermute only.
A program may use at most 64 MiB of HBM per device.

```python
import math
import jax
import jax.numpy as jnp
from jax import lax

MODES = 96
COLS = 288
CX = 128
CY = 8
CZ = 4
FACE_CAP = 128
NTYPE = 8
SECS = 16
SLABS = 16
NZ = 64


def draw_joint_count(key, part):
    upper = jax.random.randint(jax.random.fold_in(key, 11), (SLABS, SECS, SECS), FACE_CAP // 4, FACE_CAP + 1)
    upper = jnp.triu(upper, 1)
    first = jax.random.randint(jax.random.fold_in(key, 12), (), 0, SECS - 1)
    rows = jnp.arange(SECS, dtype=jnp.int32)[:, None]
    cols = jnp.arange(SECS, dtype=jnp.int32)[None, :]
    chosen = jnp.logical_and(rows == first, cols == first + 1)
    upper = jnp.where(chosen[None], FACE_CAP, upper)
    full = upper + jnp.transpose(upper, (0, 2, 1))
    return jnp.transpose(full, (1, 0, 2)).astype(jnp.int32)


def block_amplitude(key):
    level = jax.random.uniform(jax.random.fold_in(key, 21), (SECS, SLABS), jnp.float32, math.log(0.2), math.log(5.0))
    amplitude = jnp.exp(level)
    return jnp.repeat(amplitude, CZ, axis=1)[None, :, :, None, None]


def block_values(key, salt):
    shape = (MODES, SECS, NZ, CY, CX)
    noise = jnp.clip(jax.random.normal(jax.random.fold_in(key, salt), shape, jnp.float32), -6.0, 6.0)
    return (noise * block_amplitude(key)).astype(jnp.bfloat16)


def draw_modes_x(key, part):
    return block_values(key, 22)


def draw_modes_p(key, part):
    return block_values(key, 23)


def plant(array, stream_key, smallest, largest):
    place = [jax.random.randint(jax.random.fold_in(stream_key, axis), (), 0, length) for axis, length in enumerate(array.shape)]
    widest = array.shape.index(max(array.shape))
    next_to = place[:widest] + [(place[widest] + 1) % array.shape[widest]] + place[widest + 1:]
    return array.at[tuple(place)].set(smallest).at[tuple(next_to)].set(largest)


def setup_inputs(seed: int = 0) -> dict:
    key_of = jax.random.split(jax.random.key(seed), 9)
    modes_x = draw_modes_x(jax.random.fold_in(key_of[8], 71), 0)
    modes_p = draw_modes_p(jax.random.fold_in(key_of[8], 71), 0)
    ritz_values = jnp.clip(jnp.exp(jax.random.uniform(key_of[2], (MODES,), jnp.float32, math.log(0.05), math.log(2.0))), 0.05, 2.0)
    node_types = plant(jax.random.randint(key_of[3], (SECS, NZ, CY, CX), 0, NTYPE), jax.random.fold_in(key_of[3], 1), 0, NTYPE - 1).astype(jnp.int32)
    stiff_table = jnp.clip(jnp.exp(jax.random.uniform(key_of[4], (NTYPE,), jnp.float32, math.log(1.0), math.log(10.0))), 1.0, 10.0)
    mass_table = jnp.clip(jnp.exp(jax.random.uniform(key_of[5], (NTYPE,), jnp.float32, math.log(0.5), math.log(4.0))), 0.5, 4.0)
    joint_nodes = plant(jax.random.randint(key_of[6], (SECS, SLABS, SECS, FACE_CAP), 0, CZ * CY * CX), jax.random.fold_in(key_of[6], 1), 0, (CZ * CY * CX) - 1).astype(jnp.int32)
    joint_count = draw_joint_count(jax.random.fold_in(key_of[8], 71), 0)
    return {"modes_x": modes_x, "modes_p": modes_p, "ritz_values": ritz_values, "node_types": node_types, "stiff_table": stiff_table, "mass_table": mass_table, "joint_nodes": joint_nodes, "joint_count": joint_count}


JOINT_GAIN = 0.5
SPRING = (0.0, 0.1, 0.05, 0.025)
OFFSETS = [(step_z, step_y, step_x) for step_z in (-1, 0, 1) for step_y in (-1, 0, 1) for step_x in (-1, 0, 1) if (step_z, step_y, step_x) != (0, 0, 0)]

def lower_solve(lower, matrix):
    return lax.linalg.triangular_solve(lower, matrix, left_side=True, lower=True)

def edge_weights(kappa_pad):
    padded = jnp.pad(kappa_pad.astype(jnp.float32), ((0, 0), (1, 1), (1, 1)))
    depth = padded.shape[0] - 2
    height = padded.shape[1] - 2
    breadth = padded.shape[2] - 2
    centre = padded[1:-1, 1:-1, 1:-1]
    weights = []
    summed = jnp.zeros(centre.shape, jnp.float32)
    for offset in OFFSETS:
        step_z, step_y, step_x = offset
        other = padded[1 + step_z:1 + step_z + depth, 1 + step_y:1 + step_y + height, 1 + step_x:1 + step_x + breadth]
        reach = abs(step_z) + abs(step_y) + abs(step_x)
        weight = SPRING[reach] * 2.0 * centre * other / (centre + other)
        weights.append(weight)
        summed = summed + weight
    return (weights, summed)

def apply_stencil(values_pad, weights, summed):
    padded = jnp.pad(values_pad, ((0, 0), (0, 0), (1, 1), (1, 1)))
    depth = padded.shape[1] - 2
    height = padded.shape[2] - 2
    breadth = padded.shape[3] - 2
    accum = jnp.zeros((padded.shape[0], depth, height, breadth), jnp.float32)
    for offset, weight in zip(OFFSETS, weights):
        step_z, step_y, step_x = offset
        other = padded[:, 1 + step_z:1 + step_z + depth, 1 + step_y:1 + step_y + height, 1 + step_x:1 + step_x + breadth]
        accum = accum + weight[None] * other.astype(jnp.float32)
    centre = padded[:, 1:-1, 1:-1, 1:-1].astype(jnp.float32)
    return summed[None] * centre - accum

def joint_apply(result, sent, recv, node_ids, joint_w):
    width = result.shape[0]
    delta = joint_w.reshape(1, -1) * (sent.astype(jnp.float32) - recv.astype(jnp.float32)).reshape(width, -1)
    return result.reshape(width, -1).at[:, node_ids].add(delta).reshape(result.shape)

def mirror(matrix):
    return jnp.triu(matrix) + jnp.transpose(jnp.triu(matrix, 1))

def reference(modes_x, modes_p, ritz_values, node_types, stiff_table, mass_table, joint_nodes, joint_count):
    nodes = CZ * CY * CX
    kappa = jnp.take(stiff_table, node_types).astype(jnp.bfloat16)
    mass = jnp.take(mass_table, node_types)
    node_ids = joint_nodes.reshape(SECS, SLABS, SECS * FACE_CAP)
    live = (jnp.arange(FACE_CAP, dtype=jnp.int32)[None, None, None, :] < joint_count[:, :, :, None]).astype(jnp.float32)
    shifts = (jnp.arange(SLABS, dtype=jnp.int32) * nodes)[None, :, None]
    section_ids = (node_ids + shifts).reshape(SECS, SLABS * SECS * FACE_CAP)

    def faces(block):
        width = block.shape[0]
        flat = block.reshape(width, SECS, SLABS, nodes)
        sent = jnp.take_along_axis(flat, node_ids[None], axis=3).reshape(width, SECS, SLABS, SECS, FACE_CAP)
        return (sent, jnp.transpose(sent, (0, 3, 2, 1, 4)))
    kappa_sent, kappa_recv = faces(kappa[None])
    own = kappa_sent[0].astype(jnp.float32)
    other = kappa_recv[0].astype(jnp.float32)
    joint_all = JOINT_GAIN * 2.0 * own * other / (own + other) * live
    x_sent, x_recv = faces(modes_x)

    def section_setup(index):
        kappa_sec = lax.dynamic_index_in_dim(kappa, index, 0, keepdims=False)
        weights, summed = edge_weights(jnp.pad(kappa_sec, ((1, 1), (0, 0), (0, 0))))
        joint_sec = lax.dynamic_index_in_dim(joint_all, index, 0, keepdims=False)
        ids_sec = lax.dynamic_index_in_dim(section_ids, index, 0, keepdims=False)
        return (weights, summed, joint_sec, ids_sec)

    def stiffness(block, sent, recv, index, weights, summed, joint_sec, ids_sec):
        block_sec = lax.dynamic_index_in_dim(block, index, 1, keepdims=False)
        sent_sec = lax.dynamic_index_in_dim(sent, index, 1, keepdims=False)
        recv_sec = lax.dynamic_index_in_dim(recv, index, 1, keepdims=False)
        padded = jnp.pad(block_sec, ((0, 0), (1, 1), (0, 0), (0, 0)))
        result = apply_stencil(padded, weights, summed)
        return joint_apply(result, sent_sec, recv_sec, ids_sec, joint_sec)

    def first_pass(index):
        weights, summed, joint_sec, ids_sec = section_setup(index)
        diag_full = summed.reshape(-1).at[ids_sec].add(joint_sec.reshape(-1)).reshape(summed.shape)
        stiff_x = stiffness(modes_x, x_sent, x_recv, index, weights, summed, joint_sec, ids_sec)
        x_sec = lax.dynamic_index_in_dim(modes_x, index, 1, keepdims=False)
        mass_sec = lax.dynamic_index_in_dim(mass, index, 0, keepdims=False)
        resid = stiff_x - mass_sec[None] * x_sec.astype(jnp.float32) * ritz_values[:, None, None, None]
        return (resid / diag_full[None]).astype(jnp.bfloat16)
    search_sec = lax.map(first_pass, jnp.arange(SECS, dtype=jnp.int32))
    search_dir = jnp.moveaxis(search_sec, 0, 1)
    w_sent, w_recv = faces(search_dir)
    p_sent, p_recv = faces(modes_p)

    def second_pass(carry, index):
        weights, summed, joint_sec, ids_sec = section_setup(index)
        stiff_x = stiffness(modes_x, x_sent, x_recv, index, weights, summed, joint_sec, ids_sec)
        stiff_w = stiffness(search_dir, w_sent, w_recv, index, weights, summed, joint_sec, ids_sec)
        stiff_p = stiffness(modes_p, p_sent, p_recv, index, weights, summed, joint_sec, ids_sec)
        span = jnp.concatenate([lax.dynamic_index_in_dim(modes_x, index, 1, keepdims=False), lax.dynamic_index_in_dim(search_dir, index, 1, keepdims=False), lax.dynamic_index_in_dim(modes_p, index, 1, keepdims=False)], axis=0).reshape(COLS, -1)
        stiff_span = jnp.concatenate([stiff_x, stiff_w, stiff_p], axis=0).astype(jnp.bfloat16).reshape(COLS, -1)
        mass_sec = lax.dynamic_index_in_dim(mass, index, 0, keepdims=False).reshape(1, -1)
        mass_span = (mass_sec * span.astype(jnp.float32)).astype(jnp.bfloat16)
        gram_k = carry[0] + jnp.dot(span.astype(jnp.float32), jnp.transpose(stiff_span).astype(jnp.float32), preferred_element_type=jnp.float32)
        gram_m = carry[1] + jnp.dot(span.astype(jnp.float32), jnp.transpose(mass_span).astype(jnp.float32), preferred_element_type=jnp.float32)
        return ((gram_k, gram_m), None)
    zeros = jnp.zeros((COLS, COLS), jnp.float32)
    (gram_k, gram_m), unused = lax.scan(second_pass, (zeros, zeros), jnp.arange(SECS, dtype=jnp.int32))
    stiff_gram = mirror(gram_k)
    mass_gram = mirror(gram_m)
    lower = jnp.linalg.cholesky(mass_gram)
    half = lower_solve(lower, stiff_gram)
    ritz_pencil = lower_solve(lower, jnp.transpose(half))
    return (search_dir, ritz_pencil)
```

```python
import jax
import jax.numpy as jnp
from jax import lax
from jax.sharding import PartitionSpec as P

JOINT_GAIN = 0.5
SPRING = (0.0, 0.1, 0.05, 0.025)
OFFSETS = [
    (step_z, step_y, step_x)
    for step_z in (-1, 0, 1)
    for step_y in (-1, 0, 1)
    for step_x in (-1, 0, 1)
    if (step_z, step_y, step_x) != (0, 0, 0)
]


def extended(shard, sides, width):
    for axis, dim in sides:
        peers, length = (lax.axis_size(axis), shard.shape[dim])
        up = [(i, (i + 1) % peers) for i in range(peers - 1)]
        down = [(j, i) for i, j in up]
        last = lax.slice_in_dim(shard, length - width, length, axis=dim)
        first = lax.slice_in_dim(shard, 0, width, axis=dim)
        before = lax.ppermute(last, axis, up)
        after = lax.ppermute(first, axis, down)
        shard = jnp.concatenate([before, shard, after], axis=dim)
    return shard


def lower_solve(lower, matrix):
    return lax.linalg.triangular_solve(lower, matrix, left_side=True, lower=True)


def edge_weights(kappa_pad):
    padded = jnp.pad(kappa_pad.astype(jnp.float32), ((0, 0), (1, 1), (1, 1)))
    depth = padded.shape[0] - 2
    height = padded.shape[1] - 2
    breadth = padded.shape[2] - 2
    centre = padded[1:-1, 1:-1, 1:-1]
    weights = []
    summed = jnp.zeros(centre.shape, jnp.float32)
    for offset in OFFSETS:
        step_z, step_y, step_x = offset
        other = padded[
            1 + step_z : 1 + step_z + depth,
            1 + step_y : 1 + step_y + height,
            1 + step_x : 1 + step_x + breadth,
        ]
        reach = abs(step_z) + abs(step_y) + abs(step_x)
        weight = SPRING[reach] * 2.0 * centre * other / (centre + other)
        weights.append(weight)
        summed = summed + weight
    return (weights, summed)


def apply_stencil(values_pad, weights, summed):
    padded = jnp.pad(values_pad, ((0, 0), (0, 0), (1, 1), (1, 1)))
    depth = padded.shape[1] - 2
    height = padded.shape[2] - 2
    breadth = padded.shape[3] - 2
    accum = jnp.zeros((padded.shape[0], depth, height, breadth), jnp.float32)
    for offset, weight in zip(OFFSETS, weights):
        step_z, step_y, step_x = offset
        other = padded[
            :,
            1 + step_z : 1 + step_z + depth,
            1 + step_y : 1 + step_y + height,
            1 + step_x : 1 + step_x + breadth,
        ]
        accum = accum + weight[None] * other.astype(jnp.float32)
    centre = padded[:, 1:-1, 1:-1, 1:-1].astype(jnp.float32)
    return summed[None] * centre - accum


def joint_apply(result, sent, recv, node_ids, joint_w):
    width = result.shape[0]
    delta = joint_w.reshape(1, -1) * (sent.astype(jnp.float32) - recv.astype(jnp.float32)).reshape(
        width, -1
    )
    return result.reshape(width, -1).at[:, node_ids].add(delta).reshape(result.shape)


def upper_blocks(rows, cols, width):
    contract = (((1,), (1,)), ((), ()))
    parts = []
    for index in range(rows.shape[0] // width):
        part = lax.dot_general(
            rows[index * width : (index + 1) * width],
            cols[index * width :],
            contract,
            preferred_element_type=jnp.float32,
        )
        parts.append(part)
    return jnp.concatenate(parts, axis=1)


def unpack_blocks(packed, width):
    blocks = 0
    while width * blocks * (blocks + 1) // 2 < packed.shape[1]:
        blocks += 1
    offset = 0
    rows = []
    for index in range(blocks):
        span = (blocks - index) * width
        gap = jnp.zeros((width, index * width), packed.dtype)
        rows.append(jnp.concatenate([gap, packed[:, offset : offset + span]], axis=1))
        offset += span
    return jnp.concatenate(rows, axis=0)


def mirror(matrix):
    return jnp.triu(matrix) + jnp.transpose(jnp.triu(matrix, 1))


def fetch(block, node_ids, sections, capacity):
    padded = extended(block, (("bulk", 1),), 1)
    width = block.shape[0]
    sent = jnp.take(block.reshape(width, -1), node_ids, axis=1).reshape(width, sections, capacity)
    recv = lax.all_to_all(sent, "sec", split_axis=1, concat_axis=1, tiled=True)
    return (padded, sent, recv)


def on_device(
    modes_x, modes_p, ritz_values, node_types, stiff_table, mass_table, joint_nodes, joint_count
):
    modes = modes_x.shape[0]
    sections = joint_nodes.shape[2]
    capacity = joint_nodes.shape[3]
    columns = 3 * modes
    levels = jnp.arange(stiff_table.shape[0], dtype=jnp.int32)[:, None, None, None]
    chosen = node_types[0][None] == levels
    kappa = jnp.sum(jnp.where(chosen, stiff_table[:, None, None, None], 0.0), axis=0).astype(
        jnp.bfloat16
    )
    mass = jnp.sum(jnp.where(chosen, mass_table[:, None, None, None], 0.0), axis=0)
    node_ids = joint_nodes[0, 0].reshape(-1)
    live = (jnp.arange(capacity, dtype=jnp.int32)[None, :] < joint_count[0, 0][:, None]).astype(
        jnp.float32
    )
    x_local = modes_x[:, 0]
    p_local = modes_p[:, 0]
    k_row = x_local.shape[0]
    first = jnp.concatenate([x_local, kappa[None]], axis=0)
    padded, sent, recv = fetch(first, node_ids, sections, capacity)
    weights, summed = edge_weights(padded[k_row])
    own = sent[k_row].astype(jnp.float32)
    other = recv[k_row].astype(jnp.float32)
    joint_w = JOINT_GAIN * 2.0 * own * other / (own + other) * live
    diag_full = summed.reshape(-1).at[node_ids].add(joint_w.reshape(-1)).reshape(summed.shape)
    stiff_first = joint_apply(
        apply_stencil(padded[:k_row], weights, summed),
        sent[:k_row],
        recv[:k_row],
        node_ids,
        joint_w,
    )
    resid = (
        stiff_first - mass[None] * x_local.astype(jnp.float32) * ritz_values[:, None, None, None]
    )
    search_local = (resid / diag_full[None]).astype(jnp.bfloat16)
    second = jnp.concatenate([search_local, p_local], axis=0)
    padded_two, sent_two, recv_two = fetch(second, node_ids, sections, capacity)
    stiff_wp = joint_apply(
        apply_stencil(padded_two, weights, summed), sent_two, recv_two, node_ids, joint_w
    )
    span = jnp.concatenate([x_local, second], axis=0).reshape(columns, -1)
    stiff_span = (
        jnp.concatenate([stiff_first, stiff_wp], axis=0).astype(jnp.bfloat16).reshape(columns, -1)
    )
    mass_span = (mass.reshape(1, -1) * span.astype(jnp.float32)).astype(jnp.bfloat16)
    gram_m = lax.psum(lax.psum(upper_blocks(span, mass_span, modes), "bulk"), "sec")
    stiff_part = upper_blocks(span, stiff_span, modes)
    gram_m, stiff_part = lax.optimization_barrier((gram_m, stiff_part))
    gram_k = lax.psum(lax.psum(stiff_part, "bulk"), "sec")
    mass_gram = mirror(unpack_blocks(gram_m, modes))
    stiff_gram = mirror(unpack_blocks(gram_k, modes))
    lower = jnp.linalg.cholesky(mass_gram)
    inverse = lower_solve(lower, jnp.eye(columns, dtype=jnp.float32))
    exact = lax.Precision.HIGHEST
    half = jnp.matmul(inverse, stiff_gram, precision=exact)
    ritz_pencil = jnp.matmul(half, jnp.transpose(inverse), precision=exact)
    return (search_local[:, None], ritz_pencil)


def solution(mesh):
    placed = (
        P(None, "sec", "bulk", None, None),
        P(None, "sec", "bulk", None, None),
        P(),
        P("sec", "bulk", None, None),
        P(),
        P(),
        P("sec", "bulk", None, None),
        P("sec", "bulk", None),
    )
    return jax.shard_map(
        on_device,
        mesh=mesh,
        in_specs=placed,
        out_specs=(P(None, "sec", "bulk", None, None), P()),
        check_vma=False,
    )
```

```python
import jax
import jax.numpy as jnp
from jax import lax
from jax.sharding import PartitionSpec as P

JOINT_GAIN = 0.5
SPRING = (0.0, 0.1, 0.05, 0.025)
OFFSETS = [
    (step_z, step_y, step_x)
    for step_z in (-1, 0, 1)
    for step_y in (-1, 0, 1)
    for step_x in (-1, 0, 1)
    if (step_z, step_y, step_x) != (0, 0, 0)
]


def extended(shard, sides, width):
    for axis, dim in sides:
        peers, length = (lax.axis_size(axis), shard.shape[dim])
        up = [(i, (i + 1) % peers) for i in range(peers - 1)]
        down = [(j, i) for i, j in up]
        last = lax.slice_in_dim(shard, length - width, length, axis=dim)
        first = lax.slice_in_dim(shard, 0, width, axis=dim)
        before = lax.ppermute(last, axis, up)
        after = lax.ppermute(first, axis, down)
        shard = jnp.concatenate([before, shard, after], axis=dim)
    return shard


def lower_solve(lower, matrix):
    return lax.linalg.triangular_solve(lower, matrix, left_side=True, lower=True)


def edge_weights(kappa_pad):
    padded = jnp.pad(kappa_pad.astype(jnp.float32), ((0, 0), (1, 1), (1, 1)))
    depth = padded.shape[0] - 2
    height = padded.shape[1] - 2
    breadth = padded.shape[2] - 2
    centre = padded[1:-1, 1:-1, 1:-1]
    weights = []
    summed = jnp.zeros(centre.shape, jnp.float32)
    for offset in OFFSETS:
        step_z, step_y, step_x = offset
        other = padded[
            1 + step_z : 1 + step_z + depth,
            1 + step_y : 1 + step_y + height,
            1 + step_x : 1 + step_x + breadth,
        ]
        reach = abs(step_z) + abs(step_y) + abs(step_x)
        weight = SPRING[reach] * 2.0 * centre * other / (centre + other)
        weights.append(weight)
        summed = summed + weight
    return (weights, summed)


def apply_stencil(values_pad, weights, summed):
    padded = jnp.pad(values_pad, ((0, 0), (0, 0), (1, 1), (1, 1)))
    depth = padded.shape[1] - 2
    height = padded.shape[2] - 2
    breadth = padded.shape[3] - 2
    accum = jnp.zeros((padded.shape[0], depth, height, breadth), jnp.float32)
    for offset, weight in zip(OFFSETS, weights):
        step_z, step_y, step_x = offset
        other = padded[
            :,
            1 + step_z : 1 + step_z + depth,
            1 + step_y : 1 + step_y + height,
            1 + step_x : 1 + step_x + breadth,
        ]
        accum = accum + weight[None] * other.astype(jnp.float32)
    centre = padded[:, 1:-1, 1:-1, 1:-1].astype(jnp.float32)
    return summed[None] * centre - accum


def joint_apply(result, sent, recv, node_ids, joint_w):
    width = result.shape[0]
    delta = joint_w.reshape(1, -1) * (sent.astype(jnp.float32) - recv.astype(jnp.float32)).reshape(
        width, -1
    )
    return result.reshape(width, -1).at[:, node_ids].add(delta).reshape(result.shape)


def upper_blocks(rows, cols, width):
    contract = (((1,), (1,)), ((), ()))
    parts = []
    for index in range(rows.shape[0] // width):
        part = lax.dot_general(
            rows[index * width : (index + 1) * width],
            cols[index * width :],
            contract,
            preferred_element_type=jnp.float32,
        )
        parts.append(part)
    return jnp.concatenate(parts, axis=1)


def unpack_blocks(packed, width):
    blocks = 0
    while width * blocks * (blocks + 1) // 2 < packed.shape[1]:
        blocks += 1
    offset = 0
    rows = []
    for index in range(blocks):
        span = (blocks - index) * width
        gap = jnp.zeros((width, index * width), packed.dtype)
        rows.append(jnp.concatenate([gap, packed[:, offset : offset + span]], axis=1))
        offset += span
    return jnp.concatenate(rows, axis=0)


def all_sum(parts, axes):
    flat = parts.reshape(-1)
    for axis in axes:
        peers = lax.axis_size(axis)
        chunks = lax.all_to_all(flat.reshape(peers, -1), axis, 0, 0, tiled=True)
        flat = jnp.sum(chunks, axis=0)
    for axis in reversed(axes):
        peers = lax.axis_size(axis)
        copies = jnp.broadcast_to(flat[None], (peers, flat.shape[0]))
        flat = lax.all_to_all(copies, axis, 0, 0, tiled=True).reshape(-1)
    return flat.reshape(parts.shape)


def mirror(matrix):
    return jnp.triu(matrix) + jnp.transpose(jnp.triu(matrix, 1))


def fetch(block, node_ids, sections, capacity):
    padded = extended(block, (("bulk", 1),), 1)
    width = block.shape[0]
    sent = jnp.take(block.reshape(width, -1), node_ids, axis=1).reshape(width, sections, capacity)
    recv = lax.all_to_all(sent, "sec", split_axis=1, concat_axis=1, tiled=True)
    return (padded, sent, recv)


def on_device(
    modes_x, modes_p, ritz_values, node_types, stiff_table, mass_table, joint_nodes, joint_count
):
    modes = modes_x.shape[0]
    sections = joint_nodes.shape[2]
    capacity = joint_nodes.shape[3]
    columns = 3 * modes
    levels = jnp.arange(stiff_table.shape[0], dtype=jnp.int32)[:, None, None, None]
    chosen = node_types[0][None] == levels
    kappa = jnp.sum(jnp.where(chosen, stiff_table[:, None, None, None], 0.0), axis=0).astype(
        jnp.bfloat16
    )
    mass = jnp.sum(jnp.where(chosen, mass_table[:, None, None, None], 0.0), axis=0)
    node_ids = joint_nodes[0, 0].reshape(-1)
    live = (jnp.arange(capacity, dtype=jnp.int32)[None, :] < joint_count[0, 0][:, None]).astype(
        jnp.float32
    )
    x_local = modes_x[:, 0]
    p_local = modes_p[:, 0]
    k_row = x_local.shape[0]
    first = jnp.concatenate([x_local, kappa[None]], axis=0)
    padded, sent, recv = fetch(first, node_ids, sections, capacity)
    weights, summed = edge_weights(padded[k_row])
    own = sent[k_row].astype(jnp.float32)
    other = recv[k_row].astype(jnp.float32)
    joint_w = JOINT_GAIN * 2.0 * own * other / (own + other) * live
    diag_full = summed.reshape(-1).at[node_ids].add(joint_w.reshape(-1)).reshape(summed.shape)
    stiff_first = joint_apply(
        apply_stencil(padded[:k_row], weights, summed),
        sent[:k_row],
        recv[:k_row],
        node_ids,
        joint_w,
    )
    resid = (
        stiff_first - mass[None] * x_local.astype(jnp.float32) * ritz_values[:, None, None, None]
    )
    search_local = (resid / diag_full[None]).astype(jnp.bfloat16)
    second = jnp.concatenate([search_local, p_local], axis=0)
    padded_two, sent_two, recv_two = fetch(second, node_ids, sections, capacity)
    stiff_wp = joint_apply(
        apply_stencil(padded_two, weights, summed), sent_two, recv_two, node_ids, joint_w
    )
    span = jnp.concatenate([x_local, second], axis=0).reshape(columns, -1)
    stiff_span = (
        jnp.concatenate([stiff_first, stiff_wp], axis=0).astype(jnp.bfloat16).reshape(columns, -1)
    )
    mass_span = (mass.reshape(1, -1) * span.astype(jnp.float32)).astype(jnp.bfloat16)
    parts = jnp.stack(
        [upper_blocks(span, mass_span, modes), upper_blocks(span, stiff_span, modes)], axis=0
    )
    gram_m, gram_k = all_sum(parts, ("bulk", "sec"))
    mass_gram = mirror(unpack_blocks(gram_m, modes))
    stiff_gram = mirror(unpack_blocks(gram_k, modes))
    lower = jnp.linalg.cholesky(mass_gram)
    inverse = lower_solve(lower, jnp.eye(columns, dtype=jnp.float32))
    exact = lax.Precision.HIGHEST
    half = jnp.matmul(inverse, stiff_gram, precision=exact)
    ritz_pencil = jnp.matmul(half, jnp.transpose(inverse), precision=exact)
    return (search_local[:, None], ritz_pencil)


def solution(mesh):
    placed = (
        P(None, "sec", "bulk", None, None),
        P(None, "sec", "bulk", None, None),
        P(),
        P("sec", "bulk", None, None),
        P(),
        P(),
        P("sec", "bulk", None, None),
        P("sec", "bulk", None),
    )
    return jax.shard_map(
        on_device,
        mesh=mesh,
        in_specs=placed,
        out_specs=(P(None, "sec", "bulk", None, None), P()),
        check_vma=False,
    )
```

```python
import jax
import jax.numpy as jnp
from jax import lax
from jax.sharding import PartitionSpec as P

JOINT_GAIN = 0.5
SPRING = (0.0, 0.1, 0.05, 0.025)
OFFSETS = [
    (step_z, step_y, step_x)
    for step_z in (-1, 0, 1)
    for step_y in (-1, 0, 1)
    for step_x in (-1, 0, 1)
    if (step_z, step_y, step_x) != (0, 0, 0)
]


def extended(shard, sides, width):
    for axis, dim in sides:
        peers, length = (lax.axis_size(axis), shard.shape[dim])
        up = [(i, (i + 1) % peers) for i in range(peers - 1)]
        down = [(j, i) for i, j in up]
        last = lax.slice_in_dim(shard, length - width, length, axis=dim)
        first = lax.slice_in_dim(shard, 0, width, axis=dim)
        before = lax.ppermute(last, axis, up)
        after = lax.ppermute(first, axis, down)
        shard = jnp.concatenate([before, shard, after], axis=dim)
    return shard


def lower_solve(lower, matrix):
    return lax.linalg.triangular_solve(lower, matrix, left_side=True, lower=True)


def edge_weights(kappa_pad):
    padded = jnp.pad(kappa_pad.astype(jnp.float32), ((0, 0), (1, 1), (1, 1)))
    depth = padded.shape[0] - 2
    height = padded.shape[1] - 2
    breadth = padded.shape[2] - 2
    centre = padded[1:-1, 1:-1, 1:-1]
    weights = []
    summed = jnp.zeros(centre.shape, jnp.float32)
    for offset in OFFSETS:
        step_z, step_y, step_x = offset
        other = padded[
            1 + step_z : 1 + step_z + depth,
            1 + step_y : 1 + step_y + height,
            1 + step_x : 1 + step_x + breadth,
        ]
        reach = abs(step_z) + abs(step_y) + abs(step_x)
        weight = SPRING[reach] * 2.0 * centre * other / (centre + other)
        weights.append(weight)
        summed = summed + weight
    return (weights, summed)


def apply_stencil(values_pad, weights, summed):
    padded = jnp.pad(values_pad, ((0, 0), (0, 0), (1, 1), (1, 1)))
    depth = padded.shape[1] - 2
    height = padded.shape[2] - 2
    breadth = padded.shape[3] - 2
    accum = jnp.zeros((padded.shape[0], depth, height, breadth), jnp.float32)
    for offset, weight in zip(OFFSETS, weights):
        step_z, step_y, step_x = offset
        other = padded[
            :,
            1 + step_z : 1 + step_z + depth,
            1 + step_y : 1 + step_y + height,
            1 + step_x : 1 + step_x + breadth,
        ]
        accum = accum + weight[None] * other.astype(jnp.float32)
    centre = padded[:, 1:-1, 1:-1, 1:-1].astype(jnp.float32)
    return summed[None] * centre - accum


def joint_apply(result, sent, recv, node_ids, joint_w):
    width = result.shape[0]
    delta = joint_w.reshape(1, -1) * (sent.astype(jnp.float32) - recv.astype(jnp.float32)).reshape(
        width, -1
    )
    return result.reshape(width, -1).at[:, node_ids].add(delta).reshape(result.shape)


def upper_blocks(rows, cols, width):
    contract = (((1,), (1,)), ((), ()))
    parts = []
    for index in range(rows.shape[0] // width):
        part = lax.dot_general(
            rows[index * width : (index + 1) * width],
            cols[index * width :],
            contract,
            preferred_element_type=jnp.float32,
        )
        parts.append(part)
    return jnp.concatenate(parts, axis=1)


def unpack_blocks(packed, width):
    blocks = 0
    while width * blocks * (blocks + 1) // 2 < packed.shape[1]:
        blocks += 1
    offset = 0
    rows = []
    for index in range(blocks):
        span = (blocks - index) * width
        gap = jnp.zeros((width, index * width), packed.dtype)
        rows.append(jnp.concatenate([gap, packed[:, offset : offset + span]], axis=1))
        offset += span
    return jnp.concatenate(rows, axis=0)


def all_sum(parts, axes):
    flat = parts.reshape(-1)
    for axis in axes:
        peers = lax.axis_size(axis)
        chunks = lax.all_to_all(flat.reshape(peers, -1), axis, 0, 0, tiled=True)
        flat = jnp.sum(chunks, axis=0)
    for axis in reversed(axes):
        peers = lax.axis_size(axis)
        copies = jnp.broadcast_to(flat[None], (peers, flat.shape[0]))
        flat = lax.all_to_all(copies, axis, 0, 0, tiled=True).reshape(-1)
    return flat.reshape(parts.shape)


def mirror(matrix):
    return jnp.triu(matrix) + jnp.transpose(jnp.triu(matrix, 1))


def fetch(block, node_ids, sections, capacity):
    padded = extended(block, (("bulk", 1),), 1)
    width = block.shape[0]
    sent = jnp.take(block.reshape(width, -1), node_ids, axis=1).reshape(width, sections, capacity)
    recv = lax.all_to_all(sent, "sec", split_axis=1, concat_axis=1, tiled=True)
    return (padded, sent, recv)


def on_device(
    modes_x, modes_p, ritz_values, node_types, stiff_table, mass_table, joint_nodes, joint_count
):
    modes = modes_x.shape[0]
    sections = joint_nodes.shape[2]
    capacity = joint_nodes.shape[3]
    columns = 3 * modes
    levels = jnp.arange(stiff_table.shape[0], dtype=jnp.int32)[:, None, None, None]
    chosen = node_types[0][None] == levels
    kappa = jnp.sum(jnp.where(chosen, stiff_table[:, None, None, None], 0.0), axis=0).astype(
        jnp.bfloat16
    )
    mass = jnp.sum(jnp.where(chosen, mass_table[:, None, None, None], 0.0), axis=0)
    node_ids = joint_nodes[0, 0].reshape(-1)
    live = (jnp.arange(capacity, dtype=jnp.int32)[None, :] < joint_count[0, 0][:, None]).astype(
        jnp.float32
    )
    x_local = modes_x[:, 0]
    p_local = modes_p[:, 0]
    k_row = x_local.shape[0]
    first = jnp.concatenate([x_local, kappa[None]], axis=0)
    padded, sent, recv = fetch(first, node_ids, sections, capacity)
    weights, summed = edge_weights(padded[k_row])
    own = sent[k_row].astype(jnp.float32)
    other = recv[k_row].astype(jnp.float32)
    joint_w = JOINT_GAIN * 2.0 * own * other / (own + other) * live
    diag_full = summed.reshape(-1).at[node_ids].add(joint_w.reshape(-1)).reshape(summed.shape)
    stiff_first = joint_apply(
        apply_stencil(padded[:k_row], weights, summed),
        sent[:k_row],
        recv[:k_row],
        node_ids,
        joint_w,
    )
    resid = (
        stiff_first - mass[None] * x_local.astype(jnp.float32) * ritz_values[:, None, None, None]
    )
    search_local = (resid / diag_full[None]).astype(jnp.bfloat16)
    second = jnp.concatenate([search_local, p_local], axis=0)
    span = jnp.concatenate([x_local, second], axis=0).reshape(columns, -1)
    mass_span = (mass.reshape(1, -1) * span.astype(jnp.float32)).astype(jnp.bfloat16)
    gram_m = all_sum(upper_blocks(span, mass_span, modes), ("bulk", "sec"))
    mass_gram = mirror(unpack_blocks(gram_m, modes))
    lower = jnp.linalg.cholesky(mass_gram)
    inverse = lower_solve(lower, jnp.eye(columns, dtype=jnp.float32))
    padded_two, sent_two, recv_two = fetch(second, node_ids, sections, capacity)
    stiff_wp = joint_apply(
        apply_stencil(padded_two, weights, summed), sent_two, recv_two, node_ids, joint_w
    )
    stiff_span = (
        jnp.concatenate([stiff_first, stiff_wp], axis=0).astype(jnp.bfloat16).reshape(columns, -1)
    )
    gram_k = all_sum(upper_blocks(span, stiff_span, modes), ("bulk", "sec"))
    stiff_gram = mirror(unpack_blocks(gram_k, modes))
    exact = lax.Precision.HIGHEST
    half = jnp.matmul(inverse, stiff_gram, precision=exact)
    ritz_pencil = jnp.matmul(half, jnp.transpose(inverse), precision=exact)
    return (search_local[:, None], ritz_pencil)


def solution(mesh):
    placed = (
        P(None, "sec", "bulk", None, None),
        P(None, "sec", "bulk", None, None),
        P(),
        P("sec", "bulk", None, None),
        P(),
        P(),
        P("sec", "bulk", None, None),
        P("sec", "bulk", None),
    )
    return jax.shard_map(
        on_device,
        mesh=mesh,
        in_specs=placed,
        out_specs=(P(None, "sec", "bulk", None, None), P()),
        check_vma=False,
    )
```

```python
import jax
import jax.numpy as jnp
from jax import lax
from jax.sharding import PartitionSpec as P

JOINT_GAIN = 0.5
SPRING = (0.0, 0.1, 0.05, 0.025)
OFFSETS = [
    (step_z, step_y, step_x)
    for step_z in (-1, 0, 1)
    for step_y in (-1, 0, 1)
    for step_x in (-1, 0, 1)
    if (step_z, step_y, step_x) != (0, 0, 0)
]


def extended(shard, sides, width):
    for axis, dim in sides:
        peers, length = (lax.axis_size(axis), shard.shape[dim])
        up = [(i, (i + 1) % peers) for i in range(peers - 1)]
        down = [(j, i) for i, j in up]
        last = lax.slice_in_dim(shard, length - width, length, axis=dim)
        first = lax.slice_in_dim(shard, 0, width, axis=dim)
        before = lax.ppermute(last, axis, up)
        after = lax.ppermute(first, axis, down)
        shard = jnp.concatenate([before, shard, after], axis=dim)
    return shard


def lower_solve(lower, matrix):
    return lax.linalg.triangular_solve(lower, matrix, left_side=True, lower=True)


def edge_weights(kappa_pad):
    padded = jnp.pad(kappa_pad.astype(jnp.float32), ((0, 0), (1, 1), (1, 1)))
    depth = padded.shape[0] - 2
    height = padded.shape[1] - 2
    breadth = padded.shape[2] - 2
    centre = padded[1:-1, 1:-1, 1:-1]
    weights = []
    summed = jnp.zeros(centre.shape, jnp.float32)
    for offset in OFFSETS:
        step_z, step_y, step_x = offset
        other = padded[
            1 + step_z : 1 + step_z + depth,
            1 + step_y : 1 + step_y + height,
            1 + step_x : 1 + step_x + breadth,
        ]
        reach = abs(step_z) + abs(step_y) + abs(step_x)
        weight = SPRING[reach] * 2.0 * centre * other / (centre + other)
        weights.append(weight)
        summed = summed + weight
    return (weights, summed)


def apply_stencil(values_pad, weights, summed):
    padded = jnp.pad(values_pad, ((0, 0), (0, 0), (1, 1), (1, 1)))
    depth = padded.shape[1] - 2
    height = padded.shape[2] - 2
    breadth = padded.shape[3] - 2
    accum = jnp.zeros((padded.shape[0], depth, height, breadth), jnp.float32)
    for offset, weight in zip(OFFSETS, weights):
        step_z, step_y, step_x = offset
        other = padded[
            :,
            1 + step_z : 1 + step_z + depth,
            1 + step_y : 1 + step_y + height,
            1 + step_x : 1 + step_x + breadth,
        ]
        accum = accum + weight[None] * other.astype(jnp.float32)
    centre = padded[:, 1:-1, 1:-1, 1:-1].astype(jnp.float32)
    return summed[None] * centre - accum


def joint_apply(result, sent, recv, node_ids, joint_w):
    width = result.shape[0]
    delta = joint_w.reshape(1, -1) * (sent.astype(jnp.float32) - recv.astype(jnp.float32)).reshape(
        width, -1
    )
    return result.reshape(width, -1).at[:, node_ids].add(delta).reshape(result.shape)


def upper_blocks(rows, cols, width):
    contract = (((1,), (1,)), ((), ()))
    parts = []
    for index in range(rows.shape[0] // width):
        part = lax.dot_general(
            rows[index * width : (index + 1) * width],
            cols[index * width :],
            contract,
            preferred_element_type=jnp.float32,
        )
        parts.append(part)
    return jnp.concatenate(parts, axis=1)


def unpack_blocks(packed, width):
    blocks = 0
    while width * blocks * (blocks + 1) // 2 < packed.shape[1]:
        blocks += 1
    offset = 0
    rows = []
    for index in range(blocks):
        span = (blocks - index) * width
        gap = jnp.zeros((width, index * width), packed.dtype)
        rows.append(jnp.concatenate([gap, packed[:, offset : offset + span]], axis=1))
        offset += span
    return jnp.concatenate(rows, axis=0)


def all_sum(parts, axes):
    flat = parts.reshape(-1)
    for axis in axes:
        peers = lax.axis_size(axis)
        chunks = lax.all_to_all(flat.reshape(peers, -1), axis, 0, 0, tiled=True)
        flat = jnp.sum(chunks, axis=0)
    for axis in reversed(axes):
        peers = lax.axis_size(axis)
        copies = jnp.broadcast_to(flat[None], (peers, flat.shape[0]))
        flat = lax.all_to_all(copies, axis, 0, 0, tiled=True).reshape(-1)
    return flat.reshape(parts.shape)


def mirror(matrix):
    return jnp.triu(matrix) + jnp.transpose(jnp.triu(matrix, 1))


def fetch(block, node_ids, sections, capacity):
    padded = extended(block, (("bulk", 1),), 1)
    width = block.shape[0]
    sent = jnp.take(block.reshape(width, -1), node_ids, axis=1).reshape(width, sections, capacity)
    recv = lax.all_to_all(sent, "sec", split_axis=1, concat_axis=1, tiled=True)
    return (padded, sent, recv)


def on_device(
    modes_x, modes_p, ritz_values, node_types, stiff_table, mass_table, joint_nodes, joint_count
):
    modes = modes_x.shape[0]
    sections = joint_nodes.shape[2]
    capacity = joint_nodes.shape[3]
    columns = 3 * modes
    levels = jnp.arange(stiff_table.shape[0], dtype=jnp.int32)[:, None, None, None]
    chosen = node_types[0][None] == levels
    kappa = jnp.sum(jnp.where(chosen, stiff_table[:, None, None, None], 0.0), axis=0).astype(
        jnp.bfloat16
    )
    mass = jnp.sum(jnp.where(chosen, mass_table[:, None, None, None], 0.0), axis=0)
    node_ids = joint_nodes[0, 0].reshape(-1)
    live = (jnp.arange(capacity, dtype=jnp.int32)[None, :] < joint_count[0, 0][:, None]).astype(
        jnp.float32
    )
    x_local = modes_x[:, 0]
    p_local = modes_p[:, 0]
    k_row = x_local.shape[0]
    first = jnp.concatenate([x_local, kappa[None]], axis=0)
    padded, sent, recv = fetch(first, node_ids, sections, capacity)
    weights, summed = edge_weights(padded[k_row])
    own = sent[k_row].astype(jnp.float32)
    other = recv[k_row].astype(jnp.float32)
    joint_w = JOINT_GAIN * 2.0 * own * other / (own + other) * live
    stencil_first = apply_stencil(padded[:k_row], weights, summed).reshape(k_row, -1)
    delta = joint_w.reshape(1, -1) * (
        sent[:k_row].astype(jnp.float32) - recv[:k_row].astype(jnp.float32)
    ).reshape(k_row, -1)
    rows = jnp.concatenate([stencil_first, summed.reshape(1, -1)], axis=0)
    deltas = jnp.concatenate([delta, joint_w.reshape(1, -1)], axis=0)
    joined = rows.at[:, node_ids].add(deltas)
    stiff_first = joined[:k_row].reshape((k_row,) + summed.shape)
    diag_full = joined[k_row].reshape(summed.shape)
    resid = (
        stiff_first - mass[None] * x_local.astype(jnp.float32) * ritz_values[:, None, None, None]
    )
    search_local = (resid / diag_full[None]).astype(jnp.bfloat16)
    second = jnp.concatenate([search_local, p_local], axis=0)
    padded_two, sent_two, recv_two = fetch(second, node_ids, sections, capacity)
    stiff_wp = joint_apply(
        apply_stencil(padded_two, weights, summed), sent_two, recv_two, node_ids, joint_w
    )
    span = jnp.concatenate([x_local, second], axis=0).reshape(columns, -1)
    stiff_span = (
        jnp.concatenate([stiff_first, stiff_wp], axis=0).astype(jnp.bfloat16).reshape(columns, -1)
    )
    mass_span = (mass.reshape(1, -1) * span.astype(jnp.float32)).astype(jnp.bfloat16)
    parts = jnp.stack(
        [upper_blocks(span, mass_span, modes), upper_blocks(span, stiff_span, modes)], axis=0
    )
    gram_m, gram_k = all_sum(parts, ("bulk", "sec"))
    mass_gram = mirror(unpack_blocks(gram_m, modes))
    stiff_gram = mirror(unpack_blocks(gram_k, modes))
    lower = jnp.linalg.cholesky(mass_gram)
    inverse = lower_solve(lower, jnp.eye(columns, dtype=jnp.float32))
    exact = lax.Precision.HIGHEST
    half = jnp.matmul(inverse, stiff_gram, precision=exact)
    ritz_pencil = jnp.matmul(half, jnp.transpose(inverse), precision=exact)
    return (search_local[:, None], ritz_pencil)


def solution(mesh):
    placed = (
        P(None, "sec", "bulk", None, None),
        P(None, "sec", "bulk", None, None),
        P(),
        P("sec", "bulk", None, None),
        P(),
        P(),
        P("sec", "bulk", None, None),
        P("sec", "bulk", None),
    )
    return jax.shard_map(
        on_device,
        mesh=mesh,
        in_specs=placed,
        out_specs=(P(None, "sec", "bulk", None, None), P()),
        check_vma=False,
    )
```

```python
import jax
import jax.numpy as jnp
from jax import lax
from jax.sharding import PartitionSpec as P

JOINT_GAIN = 0.5
SPRING = (0.0, 0.1, 0.05, 0.025)
OFFSETS = [
    (step_z, step_y, step_x)
    for step_z in (-1, 0, 1)
    for step_y in (-1, 0, 1)
    for step_x in (-1, 0, 1)
    if (step_z, step_y, step_x) != (0, 0, 0)
]


def extended(shard, sides, width):
    for axis, dim in sides:
        peers, length = (lax.axis_size(axis), shard.shape[dim])
        up = [(i, (i + 1) % peers) for i in range(peers - 1)]
        down = [(j, i) for i, j in up]
        last = lax.slice_in_dim(shard, length - width, length, axis=dim)
        first = lax.slice_in_dim(shard, 0, width, axis=dim)
        before = lax.ppermute(last, axis, up)
        after = lax.ppermute(first, axis, down)
        shard = jnp.concatenate([before, shard, after], axis=dim)
    return shard


def lower_solve(lower, matrix):
    return lax.linalg.triangular_solve(lower, matrix, left_side=True, lower=True)


def edge_weights(kappa_pad):
    padded = jnp.pad(kappa_pad.astype(jnp.float32), ((0, 0), (1, 1), (1, 1)))
    depth = padded.shape[0] - 2
    height = padded.shape[1] - 2
    breadth = padded.shape[2] - 2
    centre = padded[1:-1, 1:-1, 1:-1]
    weights = []
    summed = jnp.zeros(centre.shape, jnp.float32)
    for offset in OFFSETS:
        step_z, step_y, step_x = offset
        other = padded[
            1 + step_z : 1 + step_z + depth,
            1 + step_y : 1 + step_y + height,
            1 + step_x : 1 + step_x + breadth,
        ]
        reach = abs(step_z) + abs(step_y) + abs(step_x)
        weight = SPRING[reach] * 2.0 * centre * other / (centre + other)
        weights.append(weight)
        summed = summed + weight
    return (weights, summed)


def apply_stencil(values_pad, weights, summed):
    padded = jnp.pad(values_pad, ((0, 0), (0, 0), (1, 1), (1, 1)))
    depth = padded.shape[1] - 2
    height = padded.shape[2] - 2
    breadth = padded.shape[3] - 2
    accum = jnp.zeros((padded.shape[0], depth, height, breadth), jnp.float32)
    for offset, weight in zip(OFFSETS, weights):
        step_z, step_y, step_x = offset
        other = padded[
            :,
            1 + step_z : 1 + step_z + depth,
            1 + step_y : 1 + step_y + height,
            1 + step_x : 1 + step_x + breadth,
        ]
        accum = accum + weight[None] * other.astype(jnp.float32)
    centre = padded[:, 1:-1, 1:-1, 1:-1].astype(jnp.float32)
    return summed[None] * centre - accum


def joint_apply(result, sent, recv, node_ids, joint_w):
    width = result.shape[0]
    delta = joint_w.reshape(1, -1) * (sent.astype(jnp.float32) - recv.astype(jnp.float32)).reshape(
        width, -1
    )
    return result.reshape(width, -1).at[:, node_ids].add(delta).reshape(result.shape)


def upper_blocks(rows, cols, width):
    contract = (((1,), (1,)), ((), ()))
    parts = []
    for index in range(rows.shape[0] // width):
        part = lax.dot_general(
            rows[index * width : (index + 1) * width],
            cols[index * width :],
            contract,
            preferred_element_type=jnp.float32,
        )
        parts.append(part)
    return jnp.concatenate(parts, axis=1)


def unpack_blocks(packed, width):
    blocks = 0
    while width * blocks * (blocks + 1) // 2 < packed.shape[1]:
        blocks += 1
    offset = 0
    rows = []
    for index in range(blocks):
        span = (blocks - index) * width
        gap = jnp.zeros((width, index * width), packed.dtype)
        rows.append(jnp.concatenate([gap, packed[:, offset : offset + span]], axis=1))
        offset += span
    return jnp.concatenate(rows, axis=0)


def all_sum(parts, axes):
    flat = parts.reshape(-1)
    for axis in axes:
        peers = lax.axis_size(axis)
        chunks = lax.all_to_all(flat.reshape(peers, -1), axis, 0, 0, tiled=True)
        flat = jnp.sum(chunks, axis=0)
    for axis in reversed(axes):
        peers = lax.axis_size(axis)
        copies = jnp.broadcast_to(flat[None], (peers, flat.shape[0]))
        flat = lax.all_to_all(copies, axis, 0, 0, tiled=True).reshape(-1)
    return flat.reshape(parts.shape)


def mirror(matrix):
    return jnp.triu(matrix) + jnp.transpose(jnp.triu(matrix, 1))


def fetch(block, node_ids, sections, capacity):
    padded = extended(block, (("bulk", 1),), 1)
    width = block.shape[0]
    sent = jnp.take(block.reshape(width, -1), node_ids, axis=1).reshape(width, sections, capacity)
    recv = lax.all_to_all(sent, "sec", split_axis=1, concat_axis=1, tiled=True)
    return (padded, sent, recv)


def on_device(
    modes_x, modes_p, ritz_values, node_types, stiff_table, mass_table, joint_nodes, joint_count
):
    modes = modes_x.shape[0]
    sections = joint_nodes.shape[2]
    capacity = joint_nodes.shape[3]
    columns = 3 * modes
    levels = jnp.arange(stiff_table.shape[0], dtype=jnp.int32)[:, None, None, None]
    chosen = node_types[0][None] == levels
    kappa = jnp.sum(jnp.where(chosen, stiff_table[:, None, None, None], 0.0), axis=0).astype(
        jnp.bfloat16
    )
    mass = jnp.sum(jnp.where(chosen, mass_table[:, None, None, None], 0.0), axis=0)
    node_ids = joint_nodes[0, 0].reshape(-1)
    live = (jnp.arange(capacity, dtype=jnp.int32)[None, :] < joint_count[0, 0][:, None]).astype(
        jnp.float32
    )
    x_local = modes_x[:, 0]
    p_local = modes_p[:, 0]
    k_row = x_local.shape[0]
    first = jnp.concatenate([x_local, kappa[None]], axis=0)
    padded, sent, recv = fetch(first, node_ids, sections, capacity)
    weights, summed = edge_weights(padded[k_row])
    own = sent[k_row].astype(jnp.float32)
    other = recv[k_row].astype(jnp.float32)
    joint_w = JOINT_GAIN * 2.0 * own * other / (own + other) * live
    stencil_first = apply_stencil(padded[:k_row], weights, summed).reshape(k_row, -1)
    delta = joint_w.reshape(1, -1) * (
        sent[:k_row].astype(jnp.float32) - recv[:k_row].astype(jnp.float32)
    ).reshape(k_row, -1)
    rows = jnp.concatenate([stencil_first, summed.reshape(1, -1)], axis=0)
    deltas = jnp.concatenate([delta, joint_w.reshape(1, -1)], axis=0)
    joined = rows.at[:, node_ids].add(deltas)
    stiff_first = joined[:k_row].reshape((k_row,) + summed.shape)
    diag_full = joined[k_row].reshape(summed.shape)
    resid = (
        stiff_first - mass[None] * x_local.astype(jnp.float32) * ritz_values[:, None, None, None]
    )
    search_local = (resid / diag_full[None]).astype(jnp.bfloat16)
    second = jnp.concatenate([search_local, p_local], axis=0)
    padded_two, sent_two, recv_two = fetch(second, node_ids, sections, capacity)
    stiff_wp = joint_apply(
        apply_stencil(padded_two, weights, summed), sent_two, recv_two, node_ids, joint_w
    )
    span = jnp.concatenate([x_local, second], axis=0).reshape(columns, -1)
    stiff_span = (
        jnp.concatenate([stiff_first, stiff_wp], axis=0).astype(jnp.bfloat16).reshape(columns, -1)
    )
    mass_span = (mass.reshape(1, -1) * span.astype(jnp.float32)).astype(jnp.bfloat16)
    parts = jnp.stack(
        [upper_blocks(span, mass_span, modes), upper_blocks(span, stiff_span, modes)], axis=0
    )
    gram_m, gram_k = all_sum(parts, (("bulk", "sec"),))
    mass_gram = mirror(unpack_blocks(gram_m, modes))
    stiff_gram = mirror(unpack_blocks(gram_k, modes))
    lower = jnp.linalg.cholesky(mass_gram)
    inverse = lower_solve(lower, jnp.eye(columns, dtype=jnp.float32))
    exact = lax.Precision.HIGHEST
    half = jnp.matmul(inverse, stiff_gram, precision=exact)
    ritz_pencil = jnp.matmul(half, jnp.transpose(inverse), precision=exact)
    return (search_local[:, None], ritz_pencil)


def solution(mesh):
    placed = (
        P(None, "sec", "bulk", None, None),
        P(None, "sec", "bulk", None, None),
        P(),
        P("sec", "bulk", None, None),
        P(),
        P(),
        P("sec", "bulk", None, None),
        P("sec", "bulk", None),
    )
    return jax.shard_map(
        on_device,
        mesh=mesh,
        in_specs=placed,
        out_specs=(P(None, "sec", "bulk", None, None), P()),
        check_vma=False,
    )
```

```python
import jax
import jax.numpy as jnp
from jax import lax
from jax.sharding import PartitionSpec as P

JOINT_GAIN = 0.5
SPRING = (0.0, 0.1, 0.05, 0.025)
OFFSETS = [
    (step_z, step_y, step_x)
    for step_z in (-1, 0, 1)
    for step_y in (-1, 0, 1)
    for step_x in (-1, 0, 1)
    if (step_z, step_y, step_x) != (0, 0, 0)
]


def extended(shard, sides, width):
    for axis, dim in sides:
        peers, length = (lax.axis_size(axis), shard.shape[dim])
        up = [(i, (i + 1) % peers) for i in range(peers - 1)]
        down = [(j, i) for i, j in up]
        last = lax.slice_in_dim(shard, length - width, length, axis=dim)
        first = lax.slice_in_dim(shard, 0, width, axis=dim)
        before = lax.ppermute(last, axis, up)
        after = lax.ppermute(first, axis, down)
        shard = jnp.concatenate([before, shard, after], axis=dim)
    return shard


def lower_solve(lower, matrix):
    return lax.linalg.triangular_solve(lower, matrix, left_side=True, lower=True)


def edge_weights(kappa_pad):
    padded = jnp.pad(kappa_pad.astype(jnp.float32), ((0, 0), (1, 1), (1, 1)))
    depth = padded.shape[0] - 2
    height = padded.shape[1] - 2
    breadth = padded.shape[2] - 2
    centre = padded[1:-1, 1:-1, 1:-1]
    weights = []
    summed = jnp.zeros(centre.shape, jnp.float32)
    for offset in OFFSETS:
        step_z, step_y, step_x = offset
        other = padded[
            1 + step_z : 1 + step_z + depth,
            1 + step_y : 1 + step_y + height,
            1 + step_x : 1 + step_x + breadth,
        ]
        reach = abs(step_z) + abs(step_y) + abs(step_x)
        weight = SPRING[reach] * 2.0 * centre * other / (centre + other)
        weights.append(weight)
        summed = summed + weight
    return (weights, summed)


def apply_stencil(values_pad, weights, summed):
    padded = jnp.pad(values_pad, ((0, 0), (0, 0), (1, 1), (1, 1)))
    depth = padded.shape[1] - 2
    height = padded.shape[2] - 2
    breadth = padded.shape[3] - 2
    accum = jnp.zeros((padded.shape[0], depth, height, breadth), jnp.float32)
    for offset, weight in zip(OFFSETS, weights):
        step_z, step_y, step_x = offset
        other = padded[
            :,
            1 + step_z : 1 + step_z + depth,
            1 + step_y : 1 + step_y + height,
            1 + step_x : 1 + step_x + breadth,
        ]
        accum = accum + weight[None] * other.astype(jnp.float32)
    centre = padded[:, 1:-1, 1:-1, 1:-1].astype(jnp.float32)
    return summed[None] * centre - accum


def joint_apply(result, sent, recv, node_ids, joint_w):
    width = result.shape[0]
    delta = joint_w.reshape(1, -1) * (sent.astype(jnp.float32) - recv.astype(jnp.float32)).reshape(
        width, -1
    )
    return result.reshape(width, -1).at[:, node_ids].add(delta).reshape(result.shape)


def upper_blocks(rows, cols, width):
    contract = (((1,), (1,)), ((), ()))
    parts = []
    for index in range(rows.shape[0] // width):
        part = lax.dot_general(
            rows[index * width : (index + 1) * width],
            cols[index * width :],
            contract,
            preferred_element_type=jnp.float32,
        )
        parts.append(part)
    return jnp.concatenate(parts, axis=1)


def unpack_blocks(packed, width):
    blocks = 0
    while width * blocks * (blocks + 1) // 2 < packed.shape[1]:
        blocks += 1
    offset = 0
    rows = []
    for index in range(blocks):
        span = (blocks - index) * width
        gap = jnp.zeros((width, index * width), packed.dtype)
        rows.append(jnp.concatenate([gap, packed[:, offset : offset + span]], axis=1))
        offset += span
    return jnp.concatenate(rows, axis=0)


def all_sum(parts, axes):
    flat = parts.reshape(-1)
    for axis in axes:
        peers = lax.axis_size(axis)
        chunks = lax.all_to_all(flat.reshape(peers, -1), axis, 0, 0, tiled=True)
        flat = jnp.sum(chunks, axis=0)
    for axis in reversed(axes):
        peers = lax.axis_size(axis)
        copies = jnp.broadcast_to(flat[None], (peers, flat.shape[0]))
        flat = lax.all_to_all(copies, axis, 0, 0, tiled=True).reshape(-1)
    return flat.reshape(parts.shape)


def factor_inverse(matrix, width):
    exact = lax.Precision.HIGHEST
    count = matrix.shape[0] // width

    def block(i, j):
        return matrix[i * width : (i + 1) * width, j * width : (j + 1) * width]

    def dot(a, b):
        return jnp.matmul(a, b, precision=exact)

    eye = jnp.eye(width, dtype=matrix.dtype)
    factor = {}
    inverse = {}
    for j in range(count):
        pivot = block(j, j)
        for t in range(j):
            pivot = pivot - dot(factor[j, t], jnp.transpose(factor[j, t]))
        factor[j, j] = jnp.linalg.cholesky(pivot)
        inverse[j, j] = lower_solve(factor[j, j], eye)
        for i in range(j + 1, count):
            panel = block(i, j)
            for t in range(j):
                panel = panel - dot(factor[i, t], jnp.transpose(factor[j, t]))
            factor[i, j] = dot(panel, jnp.transpose(inverse[j, j]))
    for j in range(count):
        for i in range(j + 1, count):
            acc = dot(factor[i, j], inverse[j, j])
            for t in range(j + 1, i):
                acc = acc + dot(factor[i, t], inverse[t, j])
            inverse[i, j] = -dot(inverse[i, i], acc)
    zero = jnp.zeros((width, width), matrix.dtype)
    rows = [
        jnp.concatenate([inverse[i, j] if j <= i else zero for j in range(count)], axis=1)
        for i in range(count)
    ]
    return jnp.concatenate(rows, axis=0)


def mirror(matrix):
    return jnp.triu(matrix) + jnp.transpose(jnp.triu(matrix, 1))


def fetch(block, node_ids, sections, capacity):
    padded = extended(block, (("bulk", 1),), 1)
    width = block.shape[0]
    sent = jnp.take(block.reshape(width, -1), node_ids, axis=1).reshape(width, sections, capacity)
    recv = lax.all_to_all(sent, "sec", split_axis=1, concat_axis=1, tiled=True)
    return (padded, sent, recv)


def on_device(
    modes_x, modes_p, ritz_values, node_types, stiff_table, mass_table, joint_nodes, joint_count
):
    modes = modes_x.shape[0]
    sections = joint_nodes.shape[2]
    capacity = joint_nodes.shape[3]
    columns = 3 * modes
    levels = jnp.arange(stiff_table.shape[0], dtype=jnp.int32)[:, None, None, None]
    chosen = node_types[0][None] == levels
    kappa = jnp.sum(jnp.where(chosen, stiff_table[:, None, None, None], 0.0), axis=0).astype(
        jnp.bfloat16
    )
    mass = jnp.sum(jnp.where(chosen, mass_table[:, None, None, None], 0.0), axis=0)
    node_ids = joint_nodes[0, 0].reshape(-1)
    live = (jnp.arange(capacity, dtype=jnp.int32)[None, :] < joint_count[0, 0][:, None]).astype(
        jnp.float32
    )
    x_local = modes_x[:, 0]
    p_local = modes_p[:, 0]
    k_row = x_local.shape[0]
    first = jnp.concatenate([x_local, kappa[None]], axis=0)
    padded, sent, recv = fetch(first, node_ids, sections, capacity)
    weights, summed = edge_weights(padded[k_row])
    own = sent[k_row].astype(jnp.float32)
    other = recv[k_row].astype(jnp.float32)
    joint_w = JOINT_GAIN * 2.0 * own * other / (own + other) * live
    stencil_first = apply_stencil(padded[:k_row], weights, summed).reshape(k_row, -1)
    delta = joint_w.reshape(1, -1) * (
        sent[:k_row].astype(jnp.float32) - recv[:k_row].astype(jnp.float32)
    ).reshape(k_row, -1)
    rows = jnp.concatenate([stencil_first, summed.reshape(1, -1)], axis=0)
    deltas = jnp.concatenate([delta, joint_w.reshape(1, -1)], axis=0)
    joined = rows.at[:, node_ids].add(deltas)
    stiff_first = joined[:k_row].reshape((k_row,) + summed.shape)
    diag_full = joined[k_row].reshape(summed.shape)
    resid = (
        stiff_first - mass[None] * x_local.astype(jnp.float32) * ritz_values[:, None, None, None]
    )
    search_local = (resid / diag_full[None]).astype(jnp.bfloat16)
    second = jnp.concatenate([search_local, p_local], axis=0)
    padded_two, sent_two, recv_two = fetch(second, node_ids, sections, capacity)
    stiff_wp = joint_apply(
        apply_stencil(padded_two, weights, summed), sent_two, recv_two, node_ids, joint_w
    )
    span = jnp.concatenate([x_local, second], axis=0).reshape(columns, -1)
    stiff_span = (
        jnp.concatenate([stiff_first, stiff_wp], axis=0).astype(jnp.bfloat16).reshape(columns, -1)
    )
    mass_span = (mass.reshape(1, -1) * span.astype(jnp.float32)).astype(jnp.bfloat16)
    parts = jnp.stack(
        [upper_blocks(span, mass_span, modes), upper_blocks(span, stiff_span, modes)], axis=0
    )
    gram_m, gram_k = all_sum(parts, (("bulk", "sec"),))
    mass_gram = mirror(unpack_blocks(gram_m, modes))
    stiff_gram = mirror(unpack_blocks(gram_k, modes))
    inverse = factor_inverse(mass_gram, modes)
    exact = lax.Precision.HIGHEST
    half = jnp.matmul(inverse, stiff_gram, precision=exact)
    ritz_pencil = jnp.matmul(half, jnp.transpose(inverse), precision=exact)
    return (search_local[:, None], ritz_pencil)


def solution(mesh):
    placed = (
        P(None, "sec", "bulk", None, None),
        P(None, "sec", "bulk", None, None),
        P(),
        P("sec", "bulk", None, None),
        P(),
        P(),
        P("sec", "bulk", None, None),
        P("sec", "bulk", None),
    )
    return jax.shard_map(
        on_device,
        mesh=mesh,
        in_specs=placed,
        out_specs=(P(None, "sec", "bulk", None, None), P()),
        check_vma=False,
    )
```

```python
import jax
import jax.numpy as jnp
from jax import lax
from jax.sharding import PartitionSpec as P

JOINT_GAIN = 0.5
SPRING = (0.0, 0.1, 0.05, 0.025)
OFFSETS = [
    (step_z, step_y, step_x)
    for step_z in (-1, 0, 1)
    for step_y in (-1, 0, 1)
    for step_x in (-1, 0, 1)
    if (step_z, step_y, step_x) != (0, 0, 0)
]


def extended(shard, sides, width):
    for axis, dim in sides:
        peers, length = (lax.axis_size(axis), shard.shape[dim])
        up = [(i, (i + 1) % peers) for i in range(peers - 1)]
        down = [(j, i) for i, j in up]
        last = lax.slice_in_dim(shard, length - width, length, axis=dim)
        first = lax.slice_in_dim(shard, 0, width, axis=dim)
        before = lax.ppermute(last, axis, up)
        after = lax.ppermute(first, axis, down)
        shard = jnp.concatenate([before, shard, after], axis=dim)
    return shard


def lower_solve(lower, matrix):
    return lax.linalg.triangular_solve(lower, matrix, left_side=True, lower=True)


def edge_weights(kappa_pad):
    padded = jnp.pad(kappa_pad.astype(jnp.float32), ((0, 0), (1, 1), (1, 1)))
    depth = padded.shape[0] - 2
    height = padded.shape[1] - 2
    breadth = padded.shape[2] - 2
    centre = padded[1:-1, 1:-1, 1:-1]
    weights = []
    summed = jnp.zeros(centre.shape, jnp.float32)
    for offset in OFFSETS:
        step_z, step_y, step_x = offset
        other = padded[
            1 + step_z : 1 + step_z + depth,
            1 + step_y : 1 + step_y + height,
            1 + step_x : 1 + step_x + breadth,
        ]
        reach = abs(step_z) + abs(step_y) + abs(step_x)
        weight = SPRING[reach] * 2.0 * centre * other / (centre + other)
        weights.append(weight)
        summed = summed + weight
    return (weights, summed)


def apply_stencil(values_pad, weights, summed):
    padded = jnp.pad(values_pad, ((0, 0), (0, 0), (1, 1), (1, 1)))
    depth = padded.shape[1] - 2
    height = padded.shape[2] - 2
    breadth = padded.shape[3] - 2
    accum = jnp.zeros((padded.shape[0], depth, height, breadth), jnp.float32)
    for offset, weight in zip(OFFSETS, weights):
        step_z, step_y, step_x = offset
        other = padded[
            :,
            1 + step_z : 1 + step_z + depth,
            1 + step_y : 1 + step_y + height,
            1 + step_x : 1 + step_x + breadth,
        ]
        accum = accum + weight[None] * other.astype(jnp.float32)
    centre = padded[:, 1:-1, 1:-1, 1:-1].astype(jnp.float32)
    return summed[None] * centre - accum


def joint_apply(result, sent, recv, node_ids, joint_w):
    width = result.shape[0]
    delta = joint_w.reshape(1, -1) * (sent.astype(jnp.float32) - recv.astype(jnp.float32)).reshape(
        width, -1
    )
    return result.reshape(width, -1).at[:, node_ids].add(delta).reshape(result.shape)


def upper_blocks(rows, cols, width):
    contract = (((1,), (1,)), ((), ()))
    parts = []
    for index in range(rows.shape[0] // width):
        part = lax.dot_general(
            rows[index * width : (index + 1) * width],
            cols[index * width :],
            contract,
            preferred_element_type=jnp.float32,
        )
        parts.append(part)
    return jnp.concatenate(parts, axis=1)


def unpack_blocks(packed, width):
    blocks = 0
    while width * blocks * (blocks + 1) // 2 < packed.shape[1]:
        blocks += 1
    offset = 0
    rows = []
    for index in range(blocks):
        span = (blocks - index) * width
        gap = jnp.zeros((width, index * width), packed.dtype)
        rows.append(jnp.concatenate([gap, packed[:, offset : offset + span]], axis=1))
        offset += span
    return jnp.concatenate(rows, axis=0)


def all_sum(parts, axes):
    flat = parts.reshape(-1)
    for axis in axes:
        peers = lax.axis_size(axis)
        chunks = lax.all_to_all(flat.reshape(peers, -1), axis, 0, 0, tiled=True)
        flat = jnp.sum(chunks, axis=0)
    for axis in reversed(axes):
        peers = lax.axis_size(axis)
        copies = jnp.broadcast_to(flat[None], (peers, flat.shape[0]))
        flat = lax.all_to_all(copies, axis, 0, 0, tiled=True).reshape(-1)
    return flat.reshape(parts.shape)


def factor_inverse(matrix, width):
    exact = lax.Precision.HIGHEST
    count = matrix.shape[0] // width

    def block(i, j):
        return matrix[i * width : (i + 1) * width, j * width : (j + 1) * width]

    def dot(a, b):
        return jnp.matmul(a, b, precision=exact)

    eye = jnp.eye(width, dtype=matrix.dtype)
    factor = {}
    inverse = {}
    for j in range(count):
        pivot = block(j, j)
        for t in range(j):
            pivot = pivot - dot(factor[j, t], jnp.transpose(factor[j, t]))
        factor[j, j] = lax.linalg.cholesky(pivot, symmetrize_input=False)
        inverse[j, j] = lower_solve(factor[j, j], eye)
        for i in range(j + 1, count):
            panel = block(i, j)
            for t in range(j):
                panel = panel - dot(factor[i, t], jnp.transpose(factor[j, t]))
            factor[i, j] = dot(panel, jnp.transpose(inverse[j, j]))
    for j in range(count):
        for i in range(j + 1, count):
            acc = dot(factor[i, j], inverse[j, j])
            for t in range(j + 1, i):
                acc = acc + dot(factor[i, t], inverse[t, j])
            inverse[i, j] = -dot(inverse[i, i], acc)
    zero = jnp.zeros((width, width), matrix.dtype)
    rows = [
        jnp.concatenate([inverse[i, j] if j <= i else zero for j in range(count)], axis=1)
        for i in range(count)
    ]
    return jnp.concatenate(rows, axis=0)


def mirror(matrix):
    return jnp.triu(matrix) + jnp.transpose(jnp.triu(matrix, 1))


def fetch(block, node_ids, sections, capacity):
    padded = extended(block, (("bulk", 1),), 1)
    width = block.shape[0]
    sent = jnp.take(block.reshape(width, -1), node_ids, axis=1).reshape(width, sections, capacity)
    recv = lax.all_to_all(sent, "sec", split_axis=1, concat_axis=1, tiled=True)
    return (padded, sent, recv)


def on_device(
    modes_x, modes_p, ritz_values, node_types, stiff_table, mass_table, joint_nodes, joint_count
):
    modes = modes_x.shape[0]
    sections = joint_nodes.shape[2]
    capacity = joint_nodes.shape[3]
    columns = 3 * modes
    levels = jnp.arange(stiff_table.shape[0], dtype=jnp.int32)[:, None, None, None]
    chosen = node_types[0][None] == levels
    kappa = jnp.sum(jnp.where(chosen, stiff_table[:, None, None, None], 0.0), axis=0).astype(
        jnp.bfloat16
    )
    mass = jnp.sum(jnp.where(chosen, mass_table[:, None, None, None], 0.0), axis=0)
    node_ids = joint_nodes[0, 0].reshape(-1)
    live = (jnp.arange(capacity, dtype=jnp.int32)[None, :] < joint_count[0, 0][:, None]).astype(
        jnp.float32
    )
    x_local = modes_x[:, 0]
    p_local = modes_p[:, 0]
    k_row = x_local.shape[0]
    first = jnp.concatenate([x_local, kappa[None]], axis=0)
    padded, sent, recv = fetch(first, node_ids, sections, capacity)
    weights, summed = edge_weights(padded[k_row])
    own = sent[k_row].astype(jnp.float32)
    other = recv[k_row].astype(jnp.float32)
    joint_w = JOINT_GAIN * 2.0 * own * other / (own + other) * live
    stencil_first = apply_stencil(padded[:k_row], weights, summed).reshape(k_row, -1)
    delta = joint_w.reshape(1, -1) * (
        sent[:k_row].astype(jnp.float32) - recv[:k_row].astype(jnp.float32)
    ).reshape(k_row, -1)
    rows = jnp.concatenate([stencil_first, summed.reshape(1, -1)], axis=0)
    deltas = jnp.concatenate([delta, joint_w.reshape(1, -1)], axis=0)
    joined = rows.at[:, node_ids].add(deltas)
    stiff_first = joined[:k_row].reshape((k_row,) + summed.shape)
    diag_full = joined[k_row].reshape(summed.shape)
    resid = (
        stiff_first - mass[None] * x_local.astype(jnp.float32) * ritz_values[:, None, None, None]
    )
    search_local = (resid / diag_full[None]).astype(jnp.bfloat16)
    second = jnp.concatenate([search_local, p_local], axis=0)
    padded_two, sent_two, recv_two = fetch(second, node_ids, sections, capacity)
    stiff_wp = joint_apply(
        apply_stencil(padded_two, weights, summed), sent_two, recv_two, node_ids, joint_w
    )
    span = jnp.concatenate([x_local, second], axis=0).reshape(columns, -1)
    stiff_span = (
        jnp.concatenate([stiff_first, stiff_wp], axis=0).astype(jnp.bfloat16).reshape(columns, -1)
    )
    mass_span = (mass.reshape(1, -1) * span.astype(jnp.float32)).astype(jnp.bfloat16)
    parts = jnp.stack(
        [upper_blocks(span, mass_span, modes), upper_blocks(span, stiff_span, modes)], axis=0
    )
    gram_m, gram_k = all_sum(parts, (("bulk", "sec"),))
    mass_gram = mirror(unpack_blocks(gram_m, modes))
    stiff_gram = mirror(unpack_blocks(gram_k, modes))
    inverse = factor_inverse(mass_gram, modes)
    exact = lax.Precision.HIGHEST
    half = jnp.matmul(inverse, stiff_gram, precision=exact)
    ritz_pencil = jnp.matmul(half, jnp.transpose(inverse), precision=exact)
    return (search_local[:, None], ritz_pencil)


def solution(mesh):
    placed = (
        P(None, "sec", "bulk", None, None),
        P(None, "sec", "bulk", None, None),
        P(),
        P("sec", "bulk", None, None),
        P(),
        P(),
        P("sec", "bulk", None, None),
        P("sec", "bulk", None),
    )
    return jax.shard_map(
        on_device,
        mesh=mesh,
        in_specs=placed,
        out_specs=(P(None, "sec", "bulk", None, None), P()),
        check_vma=False,
    )
```

```python
import jax
import jax.numpy as jnp
from jax import lax
from jax.sharding import PartitionSpec as P

JOINT_GAIN = 0.5
SPRING = (0.0, 0.1, 0.05, 0.025)
OFFSETS = [
    (step_z, step_y, step_x)
    for step_z in (-1, 0, 1)
    for step_y in (-1, 0, 1)
    for step_x in (-1, 0, 1)
    if (step_z, step_y, step_x) != (0, 0, 0)
]


def extended(shard, sides, width):
    for axis, dim in sides:
        peers, length = (lax.axis_size(axis), shard.shape[dim])
        up = [(i, (i + 1) % peers) for i in range(peers - 1)]
        down = [(j, i) for i, j in up]
        last = lax.slice_in_dim(shard, length - width, length, axis=dim)
        first = lax.slice_in_dim(shard, 0, width, axis=dim)
        before = lax.ppermute(last, axis, up)
        after = lax.ppermute(first, axis, down)
        shard = jnp.concatenate([before, shard, after], axis=dim)
    return shard


def lower_solve(lower, matrix):
    return lax.linalg.triangular_solve(lower, matrix, left_side=True, lower=True)


def edge_weights(kappa_pad):
    padded = jnp.pad(kappa_pad.astype(jnp.float32), ((0, 0), (1, 1), (1, 1)))
    depth = padded.shape[0] - 2
    height = padded.shape[1] - 2
    breadth = padded.shape[2] - 2
    centre = padded[1:-1, 1:-1, 1:-1]
    weights = []
    summed = jnp.zeros(centre.shape, jnp.float32)
    for offset in OFFSETS:
        step_z, step_y, step_x = offset
        other = padded[
            1 + step_z : 1 + step_z + depth,
            1 + step_y : 1 + step_y + height,
            1 + step_x : 1 + step_x + breadth,
        ]
        reach = abs(step_z) + abs(step_y) + abs(step_x)
        weight = SPRING[reach] * 2.0 * centre * other / (centre + other)
        weights.append(weight)
        summed = summed + weight
    return (weights, summed)


def apply_stencil(values_pad, weights, summed):
    padded = jnp.pad(values_pad, ((0, 0), (0, 0), (1, 1), (1, 1)))
    depth = padded.shape[1] - 2
    height = padded.shape[2] - 2
    breadth = padded.shape[3] - 2
    accum = jnp.zeros((padded.shape[0], depth, height, breadth), jnp.float32)
    for offset, weight in zip(OFFSETS, weights):
        step_z, step_y, step_x = offset
        other = padded[
            :,
            1 + step_z : 1 + step_z + depth,
            1 + step_y : 1 + step_y + height,
            1 + step_x : 1 + step_x + breadth,
        ]
        accum = accum + weight[None] * other.astype(jnp.float32)
    centre = padded[:, 1:-1, 1:-1, 1:-1].astype(jnp.float32)
    return summed[None] * centre - accum


def joint_apply(result, sent, recv, node_ids, joint_w):
    width = result.shape[0]
    delta = joint_w.reshape(1, -1) * (sent.astype(jnp.float32) - recv.astype(jnp.float32)).reshape(
        width, -1
    )
    return result.reshape(width, -1).at[:, node_ids].add(delta).reshape(result.shape)


def upper_blocks(rows, cols, width):
    contract = (((1,), (1,)), ((), ()))
    parts = []
    for index in range(rows.shape[0] // width):
        part = lax.dot_general(
            rows[index * width : (index + 1) * width],
            cols[index * width :],
            contract,
            preferred_element_type=jnp.float32,
        )
        parts.append(part)
    return jnp.concatenate(parts, axis=1)


def paired_blocks(rows, first, second, width):
    contract = (((1,), (1,)), ((), ()))
    left, right = [], []
    for index in range(rows.shape[0] // width):
        cols = jnp.concatenate([first[index * width :], second[index * width :]], axis=0)
        part = lax.dot_general(
            rows[index * width : (index + 1) * width],
            cols,
            contract,
            preferred_element_type=jnp.float32,
        )
        half = part.shape[1] // 2
        left.append(part[:, :half])
        right.append(part[:, half:])
    return jnp.stack([jnp.concatenate(left, axis=1), jnp.concatenate(right, axis=1)], axis=0)


def unpack_blocks(packed, width):
    blocks = 0
    while width * blocks * (blocks + 1) // 2 < packed.shape[1]:
        blocks += 1
    offset = 0
    rows = []
    for index in range(blocks):
        span = (blocks - index) * width
        gap = jnp.zeros((width, index * width), packed.dtype)
        rows.append(jnp.concatenate([gap, packed[:, offset : offset + span]], axis=1))
        offset += span
    return jnp.concatenate(rows, axis=0)


def all_sum(parts, axes):
    flat = parts.reshape(-1)
    for axis in axes:
        peers = lax.axis_size(axis)
        chunks = lax.all_to_all(flat.reshape(peers, -1), axis, 0, 0, tiled=True)
        flat = jnp.sum(chunks, axis=0)
    for axis in reversed(axes):
        peers = lax.axis_size(axis)
        copies = jnp.broadcast_to(flat[None], (peers, flat.shape[0]))
        flat = lax.all_to_all(copies, axis, 0, 0, tiled=True).reshape(-1)
    return flat.reshape(parts.shape)


def factor_inverse(matrix, width):
    exact = lax.Precision.HIGHEST
    count = matrix.shape[0] // width

    def block(i, j):
        return matrix[i * width : (i + 1) * width, j * width : (j + 1) * width]

    def dot(a, b):
        return jnp.matmul(a, b, precision=exact)

    eye = jnp.eye(width, dtype=matrix.dtype)
    factor = {}
    inverse = {}
    for j in range(count):
        pivot = block(j, j)
        for t in range(j):
            pivot = pivot - dot(factor[j, t], jnp.transpose(factor[j, t]))
        factor[j, j] = jnp.linalg.cholesky(pivot)
        inverse[j, j] = lower_solve(factor[j, j], eye)
        for i in range(j + 1, count):
            panel = block(i, j)
            for t in range(j):
                panel = panel - dot(factor[i, t], jnp.transpose(factor[j, t]))
            factor[i, j] = dot(panel, jnp.transpose(inverse[j, j]))
    for j in range(count):
        for i in range(j + 1, count):
            acc = dot(factor[i, j], inverse[j, j])
            for t in range(j + 1, i):
                acc = acc + dot(factor[i, t], inverse[t, j])
            inverse[i, j] = -dot(inverse[i, i], acc)
    zero = jnp.zeros((width, width), matrix.dtype)
    rows = [
        jnp.concatenate([inverse[i, j] if j <= i else zero for j in range(count)], axis=1)
        for i in range(count)
    ]
    return jnp.concatenate(rows, axis=0)


def mirror(matrix):
    return jnp.triu(matrix) + jnp.transpose(jnp.triu(matrix, 1))


def fetch(block, node_ids, sections, capacity):
    padded = extended(block, (("bulk", 1),), 1)
    width = block.shape[0]
    sent = jnp.take(block.reshape(width, -1), node_ids, axis=1).reshape(width, sections, capacity)
    recv = lax.all_to_all(sent, "sec", split_axis=1, concat_axis=1, tiled=True)
    return (padded, sent, recv)


def on_device(
    modes_x, modes_p, ritz_values, node_types, stiff_table, mass_table, joint_nodes, joint_count
):
    modes = modes_x.shape[0]
    sections = joint_nodes.shape[2]
    capacity = joint_nodes.shape[3]
    columns = 3 * modes
    levels = jnp.arange(stiff_table.shape[0], dtype=jnp.int32)[:, None, None, None]
    chosen = node_types[0][None] == levels
    kappa = jnp.sum(jnp.where(chosen, stiff_table[:, None, None, None], 0.0), axis=0).astype(
        jnp.bfloat16
    )
    mass = jnp.sum(jnp.where(chosen, mass_table[:, None, None, None], 0.0), axis=0)
    node_ids = joint_nodes[0, 0].reshape(-1)
    live = (jnp.arange(capacity, dtype=jnp.int32)[None, :] < joint_count[0, 0][:, None]).astype(
        jnp.float32
    )
    x_local = modes_x[:, 0]
    p_local = modes_p[:, 0]
    k_row = x_local.shape[0]
    first = jnp.concatenate([x_local, kappa[None]], axis=0)
    padded, sent, recv = fetch(first, node_ids, sections, capacity)
    weights, summed = edge_weights(padded[k_row])
    own = sent[k_row].astype(jnp.float32)
    other = recv[k_row].astype(jnp.float32)
    joint_w = JOINT_GAIN * 2.0 * own * other / (own + other) * live
    stencil_first = apply_stencil(padded[:k_row], weights, summed).reshape(k_row, -1)
    delta = joint_w.reshape(1, -1) * (
        sent[:k_row].astype(jnp.float32) - recv[:k_row].astype(jnp.float32)
    ).reshape(k_row, -1)
    rows = jnp.concatenate([stencil_first, summed.reshape(1, -1)], axis=0)
    deltas = jnp.concatenate([delta, joint_w.reshape(1, -1)], axis=0)
    joined = rows.at[:, node_ids].add(deltas)
    stiff_first = joined[:k_row].reshape((k_row,) + summed.shape)
    diag_full = joined[k_row].reshape(summed.shape)
    resid = (
        stiff_first - mass[None] * x_local.astype(jnp.float32) * ritz_values[:, None, None, None]
    )
    search_local = (resid / diag_full[None]).astype(jnp.bfloat16)
    second = jnp.concatenate([search_local, p_local], axis=0)
    padded_two, sent_two, recv_two = fetch(second, node_ids, sections, capacity)
    stiff_wp = joint_apply(
        apply_stencil(padded_two, weights, summed), sent_two, recv_two, node_ids, joint_w
    )
    span = jnp.concatenate([x_local, second], axis=0).reshape(columns, -1)
    stiff_span = (
        jnp.concatenate([stiff_first, stiff_wp], axis=0).astype(jnp.bfloat16).reshape(columns, -1)
    )
    mass_span = (mass.reshape(1, -1) * span.astype(jnp.float32)).astype(jnp.bfloat16)
    parts = paired_blocks(span, mass_span, stiff_span, modes)
    gram_m, gram_k = all_sum(parts, (("bulk", "sec"),))
    mass_gram = mirror(unpack_blocks(gram_m, modes))
    stiff_gram = mirror(unpack_blocks(gram_k, modes))
    inverse = factor_inverse(mass_gram, modes)
    exact = lax.Precision.HIGHEST
    half = jnp.matmul(inverse, stiff_gram, precision=exact)
    ritz_pencil = jnp.matmul(half, jnp.transpose(inverse), precision=exact)
    return (search_local[:, None], ritz_pencil)


def solution(mesh):
    placed = (
        P(None, "sec", "bulk", None, None),
        P(None, "sec", "bulk", None, None),
        P(),
        P("sec", "bulk", None, None),
        P(),
        P(),
        P("sec", "bulk", None, None),
        P("sec", "bulk", None),
    )
    return jax.shard_map(
        on_device,
        mesh=mesh,
        in_specs=placed,
        out_specs=(P(None, "sec", "bulk", None, None), P()),
        check_vma=False,
    )
```
